32 devices in a mesh: group: 2 (over y), seq: 4 (over z), batch: 2 (over x), chan: 2 (over core).
Axes of the slice: x: 2, y: 2, z: 4, core: 2. Of those that a mesh axis runs over, the one named last changes fastest.
Arguments:
- history: bfloat16 [8, 1024, 4096], P(('group', 'batch'), 'seq', 'chan'), parts along dimension 0, may hold values from -6 to 6
- filter_taps: bfloat16 [1024, 4096], P('seq', 'chan'), may hold values from -0.1875 to 0.1875
- lengths: int32 [8], P(('group', 'batch')), parts along dimension 0, may hold values from 256 to 1024, as said below
- inner_gate: bfloat16 [8, 256, 4096], P(('group', 'batch'), 'seq', 'chan'), parts along dimension 0, may hold values from -6 to 6
- values_in: bfloat16 [8, 256, 4096], P(('group', 'batch'), 'seq', 'chan'), parts along dimension 0, may hold values from -6 to 6
- outer_gate: bfloat16 [8, 256, 4096], P(('group', 'batch'), 'seq', 'chan'), parts along dimension 0, may hold values from -6 to 6
- skip_gain: float32 [4096], P('chan'), may hold values from -4 to 4
Outputs:
- mixed: bfloat16 [8, 256, 4096], P(('group', 'batch'), 'seq', 'chan'), parts along dimension 0
- next_history: bfloat16 [8, 1024, 4096], P(('group', 'batch'), 'seq', 'chan'), parts along dimension 0
The draws below stay inside these ranges and needn't reach their ends.
There are 2 independent parts, one for each index of `group`. The reference program is written for one: setup_inputs(seed, part) draws one part's arguments, and reference() takes and returns one part's arrays. A program takes and returns all parts, laid end to end along the dimension named above; an argument that names none is the same for every part. Nothing has to cross between parts.
Inputs may be any that keep to these rules, and one draw needn't show every extreme that they name: `lengths`: each request's prefilled length is a multiple of 256; some request of every part has exactly 1024, and some other is shorter.
All inputs are finite; a program needn't handle non-finite values.
Results may differ from the reference program's by a relative error of at most 0.0044.
Values may be sent and summed in bfloat16 or wider, within the bound.
No kernel may reach another device: no remote copies, remote signals or barrier semaphores. Data moves between devices by JAX's collectives and lax.ppermute only.
A program may use at most 128 MiB of HBM per device.

```python
import jax
import jax.numpy as jnp
from jax import lax

D = 4096
TILE = 256
SPAN = 256
REQUESTS = 4
HIST = 1024


def draw_lengths(key, part):
    first_key, second_key, third_key = jax.random.split(jax.random.fold_in(key, 7), 3)
    blocks = jax.random.randint(first_key, (REQUESTS,), 1, HIST // TILE + 1)
    chosen = jax.random.randint(second_key, (), 0, REQUESTS)
    shorter = jax.random.randint(third_key, (), 1, HIST // TILE)
    request_ids = jnp.arange(REQUESTS)
    blocks = jnp.where(request_ids == (chosen + 1) % REQUESTS, shorter, blocks)
    blocks = jnp.where(request_ids == chosen, HIST // TILE, blocks)
    return (blocks * TILE).astype(jnp.int32)


def shard_levels(rng, dims, pieces, smallest, top_value):
    loudness = 1.0
    for position, shards_of in pieces:
        heights = jax.random.uniform(jax.random.fold_in(jax.random.fold_in(rng, 6), position), (shards_of,), jnp.float32, smallest / len(pieces), top_value / len(pieces))
        loudness = loudness * jnp.repeat(jnp.exp(heights), dims[position] // shards_of).reshape((-1,) + (1,) * (len(dims) - 1 - position))
    return loudness


def bell_draw(stream_key, shape, spread, limit, shards=(), kind=jnp.bfloat16):
    result = spread * jax.random.normal(stream_key, shape, jnp.float32)
    if shards:
        result = result * shard_levels(stream_key, shape, shards, -0.22, 0.18)
    return jnp.clip(result, -limit, limit).astype(kind)


def setup_inputs(seed: int = 0, part: int = 0) -> dict:
    key_of = jax.random.split(jax.random.key(seed), 8)
    own_keys = jax.random.split(jax.random.fold_in(key_of[7], part), 8)
    history = bell_draw(own_keys[0], (REQUESTS, HIST, D), 1.0, 6.0, ((0, 2), (1, 4), (2, 2)))
    filter_taps = bell_draw(key_of[1], (HIST, D), HIST ** -0.5, 0.1875, ((0, 4), (1, 2)))
    lengths = draw_lengths(jax.random.fold_in(jax.random.fold_in(key_of[7], part), 71), part)
    inner_gate = bell_draw(own_keys[3], (REQUESTS, SPAN, D), 1.0, 6.0, ((0, 2), (1, 4), (2, 2)))
    values_in = bell_draw(own_keys[4], (REQUESTS, SPAN, D), 1.0, 6.0, ((0, 2), (1, 4), (2, 2)))
    outer_gate = bell_draw(own_keys[5], (REQUESTS, SPAN, D), 1.0, 6.0, ((0, 2), (1, 4), (2, 2)))
    skip_gain = bell_draw(key_of[6], (D,), 1.0, 4.0, ((0, 2),), jnp.float32)
    return {"history": history, "filter_taps": filter_taps, "lengths": lengths, "inner_gate": inner_gate, "values_in": values_in, "outer_gate": outer_gate, "skip_gain": skip_gain}


def correlate(signal, kernel, count):
    total = signal.shape[0] + kernel.shape[0]
    left = jnp.fft.rfft(signal, total, axis=0)
    right = jnp.fft.rfft(kernel, total, axis=0)
    return jnp.fft.irfft(left * jnp.conj(right), total, axis=0)[:count]


def reference(history, filter_taps, lengths, inner_gate, values_in, outer_gate, skip_gain):
    product = (inner_gate.astype(jnp.float32) * values_in.astype(jnp.float32)).astype(jnp.bfloat16)
    taps = filter_taps.astype(jnp.float32)
    padded_taps = jnp.concatenate([taps, jnp.zeros((SPAN, D), taps.dtype)], axis=0)[1:]
    reversed_front = taps[:SPAN][::-1]
    lag_ids = jnp.arange(HIST, dtype=jnp.int32)

    def one_request(items):
        cache_rows, length, product_rows, outer_rows = items
        live_rows = jnp.where((lag_ids < length)[:, None], cache_rows, jnp.zeros_like(cache_rows))
        hist_term = correlate(padded_taps, live_rows.astype(jnp.float32), SPAN)
        recent_in = product_rows.astype(jnp.float32)
        window = jnp.concatenate([jnp.zeros((SPAN, D), recent_in.dtype), recent_in], axis=0)[1:]
        new_term = correlate(window, reversed_front, SPAN)
        total = hist_term + new_term + skip_gain[None, :] * recent_in
        return (outer_rows.astype(jnp.float32) * total).astype(jnp.bfloat16)

    mixed = lax.map(one_request, (history, lengths, product, outer_gate))
    next_history = jnp.concatenate([product[:, ::-1], history[:, :HIST - SPAN]], axis=1)
    return mixed, next_history
```

```python
import jax
import jax.numpy as jnp
from jax import lax
from jax.sharding import PartitionSpec as P


def from_behind(block, axis, distance):
    devices = range(lax.axis_size(axis))
    route = [(i - distance, i) for i in devices if i - distance in devices]
    return lax.ppermute(block, axis, route)


def correlate(signal, kernel):
    width = signal.shape[2]
    return lax.conv_general_dilated(
        signal,
        kernel[:, None, :],
        (1,),
        "VALID",
        dimension_numbers=("NWC", "WIO", "NWC"),
        feature_group_count=width,
        preferred_element_type=jnp.float32,
    )


def per_device(history, filter_taps, lengths, inner_gate, values_in, outer_gate, skip_gain):
    position = lax.axis_index("seq")
    n_seq = lax.axis_size("seq")
    requests, tile_len, width = history.shape
    own_tokens = inner_gate.shape[1]
    span_len = own_tokens * n_seq
    assert span_len == tile_len
    step = own_tokens
    product_own = (inner_gate.astype(jnp.float32) * values_in.astype(jnp.float32)).astype(
        jnp.bfloat16
    )
    product_all = lax.all_gather(product_own, "seq", axis=1, tiled=True)
    head_product = product_all[:, ::-1]
    row_ids = position * tile_len + jnp.arange(tile_len, dtype=jnp.int32)
    live_rows = jnp.where(
        (row_ids[None, :] < lengths[:, None])[:, :, None], history, jnp.zeros_like(history)
    )
    prev_keep = ((row_ids - tile_len)[None, :] < lengths[:, None])[:, :, None]

    head_parts = []
    prev_live = []
    sums = []
    for c in range(n_seq):
        lo = tile_len - step * (c + 1)
        hi = lo + step
        sent = from_behind(history[:, lo:hi], "seq", 1)
        if c == 0:
            first = product_own[:, ::-1]
        else:
            first = head_product[:, lo:hi]
        head_c = jnp.where(position == 0, first, sent)
        head_parts.append(head_c)
        prev_live.insert(
            0, jnp.where(prev_keep[:, lo:hi], head_c, jnp.zeros_like(head_c))
        )
        segment = jnp.concatenate(prev_live + [live_rows[:, : hi - 1]], axis=1)
        partial_rev = correlate(segment, filter_taps)
        sums.append(lax.psum(partial_rev, "seq"))
    own_rev = jnp.stack(sums)[position]
    summed = own_rev[:, ::-1]
    product_float = product_own.astype(jnp.float32)
    total = summed + skip_gain[None, None, :] * product_float
    mixed = (outer_gate.astype(jnp.float32) * total).astype(jnp.bfloat16)
    next_history = jnp.concatenate(head_parts[::-1], axis=1)
    return (mixed, next_history)


def solution(mesh):
    in_specs = (
        P(("group", "batch"), "seq", "chan"),
        P("seq", "chan"),
        P(("group", "batch")),
        P(("group", "batch"), "seq", "chan"),
        P(("group", "batch"), "seq", "chan"),
        P(("group", "batch"), "seq", "chan"),
        P("chan"),
    )
    out_specs = (P(("group", "batch"), "seq", "chan"), P(("group", "batch"), "seq", "chan"))
    return jax.shard_map(
        per_device, mesh=mesh, in_specs=in_specs, out_specs=out_specs, check_vma=False
    )
```

```python
import jax
import jax.numpy as jnp
from jax import lax
from jax.sharding import PartitionSpec as P


def from_behind(block, axis, distance):
    devices = range(lax.axis_size(axis))
    route = [(i - distance, i) for i in devices if i - distance in devices]
    return lax.ppermute(block, axis, route)


def correlate(signal, kernel):
    width = signal.shape[2]
    return lax.conv_general_dilated(
        signal,
        kernel[:, None, :],
        (1,),
        "VALID",
        dimension_numbers=("NWC", "WIO", "NWC"),
        feature_group_count=width,
        preferred_element_type=jnp.float32,
    )


def per_device(history, filter_taps, lengths, inner_gate, values_in, outer_gate, skip_gain):
    position = lax.axis_index("seq")
    n_seq = lax.axis_size("seq")
    requests, tile_len, width = history.shape
    own_tokens = inner_gate.shape[1]
    span_len = own_tokens * n_seq
    assert span_len == tile_len
    step = own_tokens
    product_own = (inner_gate.astype(jnp.float32) * values_in.astype(jnp.float32)).astype(
        jnp.bfloat16
    )
    product_rev = (
        inner_gate[:, ::-1].astype(jnp.float32) * values_in[:, ::-1].astype(jnp.float32)
    ).astype(jnp.bfloat16)
    row_ids = position * tile_len + jnp.arange(tile_len, dtype=jnp.int32)
    live_rows = jnp.where(
        (row_ids[None, :] < lengths[:, None])[:, :, None], history, jnp.zeros_like(history)
    )
    prev_keep = ((row_ids - tile_len)[None, :] < lengths[:, None])[:, :, None]

    head_parts = []
    prev_live = []
    sums = []
    for c in range(n_seq):
        lo = tile_len - step * (c + 1)
        hi = lo + step
        sent = from_behind(history[:, lo:hi], "seq", 1)
        if c == 0:
            first = product_rev
        else:
            first = lax.ppermute(product_rev, "seq", [(c, 0)])
        if sums:
            (sent, first), _ = lax.optimization_barrier(((sent, first), last_partial))
        head_c = jnp.where(position == 0, first, sent)
        head_parts.append(head_c)
        prev_live.insert(
            0, jnp.where(prev_keep[:, lo:hi], head_c, jnp.zeros_like(head_c))
        )
        segment = jnp.concatenate(prev_live + [live_rows[:, : hi - 1]], axis=1)
        partial_rev = correlate(segment, filter_taps)
        last_partial = partial_rev
        if sums:
            partial_rev, _ = lax.optimization_barrier((partial_rev, sums[-1]))
        sums.append(lax.psum(partial_rev, "seq"))
    own_rev = jnp.stack(sums)[position]
    summed = own_rev[:, ::-1]
    product_float = product_own.astype(jnp.float32)
    total = summed + skip_gain[None, None, :] * product_float
    mixed = (outer_gate.astype(jnp.float32) * total).astype(jnp.bfloat16)
    next_history = jnp.concatenate(head_parts[::-1], axis=1)
    return (mixed, next_history)


def solution(mesh):
    in_specs = (
        P(("group", "batch"), "seq", "chan"),
        P("seq", "chan"),
        P(("group", "batch")),
        P(("group", "batch"), "seq", "chan"),
        P(("group", "batch"), "seq", "chan"),
        P(("group", "batch"), "seq", "chan"),
        P("chan"),
    )
    out_specs = (P(("group", "batch"), "seq", "chan"), P(("group", "batch"), "seq", "chan"))
    return jax.shard_map(
        per_device, mesh=mesh, in_specs=in_specs, out_specs=out_specs, check_vma=False
    )
```

```python
import jax
import jax.numpy as jnp
from jax import lax
from jax.sharding import PartitionSpec as P

CHANNEL_CHUNKS = 4


def from_behind(block, axis, distance):
    devices = range(lax.axis_size(axis))
    route = [(i - distance, i) for i in devices if i - distance in devices]
    return lax.ppermute(block, axis, route)


def correlate(signal, kernel):
    width = signal.shape[2]
    return lax.conv_general_dilated(
        signal,
        kernel[:, None, :],
        (1,),
        "VALID",
        dimension_numbers=("NWC", "WIO", "NWC"),
        feature_group_count=width,
        preferred_element_type=jnp.float32,
    )


def per_device(history, filter_taps, lengths, inner_gate, values_in, outer_gate, skip_gain):
    position = lax.axis_index("seq")
    n_seq = lax.axis_size("seq")
    requests, tile_len, width = history.shape
    own_tokens = inner_gate.shape[1]
    span_len = own_tokens * n_seq
    assert span_len == tile_len
    chunk = width // CHANNEL_CHUNKS
    product_own = (inner_gate.astype(jnp.float32) * values_in.astype(jnp.float32)).astype(
        jnp.bfloat16
    )
    product_rev = (
        inner_gate[:, ::-1].astype(jnp.float32) * values_in[:, ::-1].astype(jnp.float32)
    ).astype(jnp.bfloat16)
    product_own, product_rev = lax.optimization_barrier((product_own, product_rev))
    gathered = lax.all_gather(product_rev, "seq", axis=1, tiled=True)
    head_product = gathered.reshape(requests, n_seq, own_tokens, width)[:, ::-1].reshape(
        requests, tile_len, width
    )
    row_ids = position * tile_len + jnp.arange(tile_len, dtype=jnp.int32)
    live_rows = jnp.where(
        (row_ids[None, :] < lengths[:, None])[:, :, None], history, jnp.zeros_like(history)
    )
    prev_keep = ((row_ids - tile_len)[None, :] < lengths[:, None])[:, :, None]

    head_parts = []
    own_parts = []
    for c in range(CHANNEL_CHUNKS):
        cols = slice(c * chunk, (c + 1) * chunk)
        sent = from_behind(history[:, :, cols], "seq", 1)
        if own_parts:
            sent, _ = lax.optimization_barrier((sent, last_partial))
        head_c = jnp.where(position == 0, head_product[:, :, cols], sent)
        head_parts.append(head_c)
        prev_live = jnp.where(prev_keep, head_c, jnp.zeros_like(head_c))
        segment = jnp.concatenate([prev_live, live_rows[:, : tile_len - 1, cols]], axis=1)
        partial_rev = correlate(segment, filter_taps[:, cols])
        last_partial = partial_rev
        blocks = partial_rev.reshape(requests, n_seq, own_tokens, chunk)[:, ::-1]
        if own_parts:
            blocks, _ = lax.optimization_barrier((blocks, own_parts[-1]))
        reduced = lax.psum_scatter(blocks, "seq", scatter_dimension=1, tiled=True)
        own_parts.append(reduced[:, 0])
    summed = jnp.concatenate(own_parts, axis=2)[:, ::-1]
    product_float = product_own.astype(jnp.float32)
    total = summed + skip_gain[None, None, :] * product_float
    mixed = (outer_gate.astype(jnp.float32) * total).astype(jnp.bfloat16)
    next_history = jnp.concatenate(head_parts, axis=2)
    return (mixed, next_history)


def solution(mesh):
    in_specs = (
        P(("group", "batch"), "seq", "chan"),
        P("seq", "chan"),
        P(("group", "batch")),
        P(("group", "batch"), "seq", "chan"),
        P(("group", "batch"), "seq", "chan"),
        P(("group", "batch"), "seq", "chan"),
        P("chan"),
    )
    out_specs = (P(("group", "batch"), "seq", "chan"), P(("group", "batch"), "seq", "chan"))
    return jax.shard_map(
        per_device, mesh=mesh, in_specs=in_specs, out_specs=out_specs, check_vma=False
    )
```

```python
import jax
import jax.numpy as jnp
from jax import lax
from jax.sharding import PartitionSpec as P

CHANNEL_CHUNKS = 4


def from_behind(block, axis, distance):
    devices = range(lax.axis_size(axis))
    route = [(i - distance, i) for i in devices if i - distance in devices]
    return lax.ppermute(block, axis, route)


def correlate(signal, kernel):
    width = signal.shape[2]
    return lax.conv_general_dilated(
        signal,
        kernel[:, None, :],
        (1,),
        "VALID",
        dimension_numbers=("NWC", "WIO", "NWC"),
        feature_group_count=width,
        preferred_element_type=jnp.float32,
    )


def per_device(history, filter_taps, lengths, inner_gate, values_in, outer_gate, skip_gain):
    position = lax.axis_index("seq")
    n_seq = lax.axis_size("seq")
    requests, tile_len, width = history.shape
    own_tokens = inner_gate.shape[1]
    span_len = own_tokens * n_seq
    assert span_len == tile_len
    chunk = width // CHANNEL_CHUNKS
    product_own = (inner_gate.astype(jnp.float32) * values_in.astype(jnp.float32)).astype(
        jnp.bfloat16
    )
    token_ids = jnp.arange(own_tokens, dtype=jnp.int32)
    exchange = (token_ids[:, None] + token_ids[None, :] == own_tokens - 1).astype(jnp.bfloat16)
    product_own = lax.optimization_barrier(product_own)
    product_rev = jnp.einsum(
        "ik,rkc->ric", exchange, product_own, preferred_element_type=jnp.float32
    ).astype(jnp.bfloat16)
    from_each = [product_rev] + [
        lax.ppermute(product_rev, "seq", [(d, 0)]) for d in range(1, n_seq)
    ]
    row_ids = position * tile_len + jnp.arange(tile_len, dtype=jnp.int32)
    live_rows = jnp.where(
        (row_ids[None, :] < lengths[:, None])[:, :, None], history, jnp.zeros_like(history)
    )
    prev_keep = ((row_ids - tile_len)[None, :] < lengths[:, None])[:, :, None]

    head_parts = []
    own_parts = []
    for c in range(CHANNEL_CHUNKS):
        cols = slice(c * chunk, (c + 1) * chunk)
        sent = from_behind(history[:, :, cols], "seq", 1)
        if own_parts:
            sent, _ = lax.optimization_barrier((sent, last_partial))
        head_first = jnp.concatenate([part[:, :, cols] for part in from_each[::-1]], axis=1)
        head_c = jnp.where(position == 0, head_first, sent)
        head_parts.append(head_c)
        prev_live = jnp.where(prev_keep, head_c, jnp.zeros_like(head_c))
        segment = jnp.concatenate([prev_live, live_rows[:, : tile_len - 1, cols]], axis=1)
        partial_rev = correlate(segment, filter_taps[:, cols])
        last_partial = partial_rev
        blocks = partial_rev.reshape(requests, n_seq, own_tokens, chunk)[:, ::-1]
        if own_parts:
            blocks, _ = lax.optimization_barrier((blocks, own_parts[-1]))
        reduced = lax.psum_scatter(blocks, "seq", scatter_dimension=1, tiled=True)
        own_parts.append(reduced[:, 0])
    summed = jnp.concatenate(own_parts, axis=2)[:, ::-1]
    product_float = product_own.astype(jnp.float32)
    total = summed + skip_gain[None, None, :] * product_float
    mixed = (outer_gate.astype(jnp.float32) * total).astype(jnp.bfloat16)
    next_history = jnp.concatenate(head_parts, axis=2)
    return (mixed, next_history)


def solution(mesh):
    in_specs = (
        P(("group", "batch"), "seq", "chan"),
        P("seq", "chan"),
        P(("group", "batch")),
        P(("group", "batch"), "seq", "chan"),
        P(("group", "batch"), "seq", "chan"),
        P(("group", "batch"), "seq", "chan"),
        P("chan"),
    )
    out_specs = (P(("group", "batch"), "seq", "chan"), P(("group", "batch"), "seq", "chan"))
    return jax.shard_map(
        per_device, mesh=mesh, in_specs=in_specs, out_specs=out_specs, check_vma=False
    )
```

```python
import jax
import jax.numpy as jnp
from jax import lax
from jax.sharding import PartitionSpec as P

CHANNEL_CHUNKS = 4


def from_behind(block, axis, distance):
    devices = range(lax.axis_size(axis))
    route = [(i - distance, i) for i in devices if i - distance in devices]
    return lax.ppermute(block, axis, route)


def correlate(signal, kernel):
    width = signal.shape[2]
    return lax.conv_general_dilated(
        signal,
        kernel[:, None, :],
        (1,),
        "VALID",
        dimension_numbers=("NWC", "WIO", "NWC"),
        feature_group_count=width,
        preferred_element_type=jnp.float32,
    )


def per_device(history, filter_taps, lengths, inner_gate, values_in, outer_gate, skip_gain):
    position = lax.axis_index("seq")
    n_seq = lax.axis_size("seq")
    requests, tile_len, width = history.shape
    own_tokens = inner_gate.shape[1]
    span_len = own_tokens * n_seq
    assert span_len == tile_len
    chunk = width // CHANNEL_CHUNKS
    product_own = (inner_gate.astype(jnp.float32) * values_in.astype(jnp.float32)).astype(
        jnp.bfloat16
    )
    token_ids = jnp.arange(own_tokens, dtype=jnp.int32)
    exchange = (token_ids[:, None] + token_ids[None, :] == own_tokens - 1).astype(jnp.bfloat16)
    product_own = lax.optimization_barrier(product_own)
    product_rev = jnp.einsum(
        "ik,rkc->ric", exchange, product_own, preferred_element_type=jnp.float32
    ).astype(jnp.bfloat16)
    first_each = [product_rev[:, :, :chunk]] + [
        lax.ppermute(product_rev[:, :, :chunk], "seq", [(d, 0)]) for d in range(1, n_seq)
    ]
    rest_each = [product_rev[:, :, chunk:]] + [
        lax.ppermute(product_rev[:, :, chunk:], "seq", [(d, 0)]) for d in range(1, n_seq)
    ]
    row_ids = position * tile_len + jnp.arange(tile_len, dtype=jnp.int32)
    live_rows = jnp.where(
        (row_ids[None, :] < lengths[:, None])[:, :, None], history, jnp.zeros_like(history)
    )
    prev_keep = ((row_ids - tile_len)[None, :] < lengths[:, None])[:, :, None]

    head_parts = []
    own_parts = []
    for c in range(CHANNEL_CHUNKS):
        cols = slice(c * chunk, (c + 1) * chunk)
        sent = from_behind(history[:, :, cols], "seq", 1)
        if own_parts:
            (sent, rest_each), _ = lax.optimization_barrier(((sent, rest_each), last_partial))
            rest_cols = slice((c - 1) * chunk, c * chunk)
            head_first = jnp.concatenate(
                [part[:, :, rest_cols] for part in rest_each[::-1]], axis=1
            )
        else:
            head_first = jnp.concatenate(first_each[::-1], axis=1)
        head_c = jnp.where(position == 0, head_first, sent)
        head_parts.append(head_c)
        prev_live = jnp.where(prev_keep, head_c, jnp.zeros_like(head_c))
        segment = jnp.concatenate([prev_live, live_rows[:, : tile_len - 1, cols]], axis=1)
        partial_rev = correlate(segment, filter_taps[:, cols])
        last_partial = partial_rev
        blocks = partial_rev.reshape(requests, n_seq, own_tokens, chunk)[:, ::-1]
        if own_parts:
            blocks, _ = lax.optimization_barrier((blocks, own_parts[-1]))
        reduced = lax.psum_scatter(blocks, "seq", scatter_dimension=1, tiled=True)
        own_parts.append(reduced[:, 0])
    summed = jnp.concatenate(own_parts, axis=2)[:, ::-1]
    product_float = product_own.astype(jnp.float32)
    total = summed + skip_gain[None, None, :] * product_float
    mixed = (outer_gate.astype(jnp.float32) * total).astype(jnp.bfloat16)
    next_history = jnp.concatenate(head_parts, axis=2)
    return (mixed, next_history)


def solution(mesh):
    in_specs = (
        P(("group", "batch"), "seq", "chan"),
        P("seq", "chan"),
        P(("group", "batch")),
        P(("group", "batch"), "seq", "chan"),
        P(("group", "batch"), "seq", "chan"),
        P(("group", "batch"), "seq", "chan"),
        P("chan"),
    )
    out_specs = (P(("group", "batch"), "seq", "chan"), P(("group", "batch"), "seq", "chan"))
    return jax.shard_map(
        per_device, mesh=mesh, in_specs=in_specs, out_specs=out_specs, check_vma=False
    )
```

```python
import jax
import jax.numpy as jnp
from jax import lax
from jax.sharding import PartitionSpec as P

CHUNK_PARTS = (2, 4, 4, 4, 2)


def from_behind(block, axis, distance):
    devices = range(lax.axis_size(axis))
    route = [(i - distance, i) for i in devices if i - distance in devices]
    return lax.ppermute(block, axis, route)


def correlate(signal, kernel):
    width = signal.shape[2]
    return lax.conv_general_dilated(
        signal,
        kernel[:, None, :],
        (1,),
        "VALID",
        dimension_numbers=("NWC", "WIO", "NWC"),
        feature_group_count=width,
        preferred_element_type=jnp.float32,
    )


def per_device(history, filter_taps, lengths, inner_gate, values_in, outer_gate, skip_gain):
    position = lax.axis_index("seq")
    n_seq = lax.axis_size("seq")
    requests, tile_len, width = history.shape
    own_tokens = inner_gate.shape[1]
    span_len = own_tokens * n_seq
    assert span_len == tile_len
    unit = width // sum(CHUNK_PARTS)
    bounds = [0]
    for parts in CHUNK_PARTS:
        bounds.append(bounds[-1] + parts * unit)
    chunk = bounds[1]
    product_own = (inner_gate.astype(jnp.float32) * values_in.astype(jnp.float32)).astype(
        jnp.bfloat16
    )
    token_ids = jnp.arange(own_tokens, dtype=jnp.int32)
    exchange = (token_ids[:, None] + token_ids[None, :] == own_tokens - 1).astype(jnp.bfloat16)
    product_own = lax.optimization_barrier(product_own)
    product_rev = jnp.einsum(
        "ik,rkc->ric", exchange, product_own, preferred_element_type=jnp.float32
    ).astype(jnp.bfloat16)
    first_each = [product_rev[:, :, :chunk]] + [
        lax.ppermute(product_rev[:, :, :chunk], "seq", [(d, 0)]) for d in range(1, n_seq)
    ]
    rest_each = [product_rev[:, :, chunk:]] + [
        lax.ppermute(product_rev[:, :, chunk:], "seq", [(d, 0)]) for d in range(1, n_seq)
    ]
    row_ids = position * tile_len + jnp.arange(tile_len, dtype=jnp.int32)
    live_rows = jnp.where(
        (row_ids[None, :] < lengths[:, None])[:, :, None], history, jnp.zeros_like(history)
    )
    prev_keep = ((row_ids - tile_len)[None, :] < lengths[:, None])[:, :, None]

    head_parts = []
    own_parts = []
    for c in range(len(CHUNK_PARTS)):
        cols = slice(bounds[c], bounds[c + 1])
        sent = from_behind(history[:, :, cols], "seq", 1)
        if own_parts:
            (sent, rest_each), _ = lax.optimization_barrier(((sent, rest_each), last_partial))
            rest_cols = slice(bounds[c] - chunk, bounds[c + 1] - chunk)
            head_first = jnp.concatenate(
                [part[:, :, rest_cols] for part in rest_each[::-1]], axis=1
            )
        else:
            head_first = jnp.concatenate(first_each[::-1], axis=1)
        head_c = jnp.where(position == 0, head_first, sent)
        head_parts.append(head_c)
        prev_live = jnp.where(prev_keep, head_c, jnp.zeros_like(head_c))
        segment = jnp.concatenate([prev_live, live_rows[:, : tile_len - 1, cols]], axis=1)
        partial_rev = correlate(segment, filter_taps[:, cols])
        last_partial = partial_rev
        blocks = partial_rev.reshape(requests, n_seq, own_tokens, -1)[:, ::-1]
        if own_parts:
            blocks, _ = lax.optimization_barrier((blocks, own_parts[-1]))
        reduced = lax.psum_scatter(blocks, "seq", scatter_dimension=1, tiled=True)
        own_parts.append(reduced[:, 0])
    summed = jnp.concatenate(own_parts, axis=2)[:, ::-1]
    product_float = product_own.astype(jnp.float32)
    total = summed + skip_gain[None, None, :] * product_float
    mixed = (outer_gate.astype(jnp.float32) * total).astype(jnp.bfloat16)
    next_history = jnp.concatenate(head_parts, axis=2)
    return (mixed, next_history)


def solution(mesh):
    in_specs = (
        P(("group", "batch"), "seq", "chan"),
        P("seq", "chan"),
        P(("group", "batch")),
        P(("group", "batch"), "seq", "chan"),
        P(("group", "batch"), "seq", "chan"),
        P(("group", "batch"), "seq", "chan"),
        P("chan"),
    )
    out_specs = (P(("group", "batch"), "seq", "chan"), P(("group", "batch"), "seq", "chan"))
    return jax.shard_map(
        per_device, mesh=mesh, in_specs=in_specs, out_specs=out_specs, check_vma=False
    )
```

```python
import jax
import jax.numpy as jnp
from jax import lax
from jax.sharding import PartitionSpec as P

CHANNEL_CHUNKS = 4


def from_behind(block, axis, distance):
    devices = range(lax.axis_size(axis))
    route = [(i - distance, i) for i in devices if i - distance in devices]
    return lax.ppermute(block, axis, route)


def send_reduce(blocks, position, n_seq):
    total = lax.dynamic_index_in_dim(blocks, position, axis=1, keepdims=False)
    for shift in range(1, n_seq):
        piece = lax.dynamic_index_in_dim(blocks, (position + shift) % n_seq, axis=1, keepdims=False)
        route = [(p, (p + shift) % n_seq) for p in range(n_seq)]
        total = total + lax.ppermute(piece, "seq", route)
    return total


def correlate(signal, kernel):
    width = signal.shape[2]
    return lax.conv_general_dilated(
        signal,
        kernel[:, None, :],
        (1,),
        "VALID",
        dimension_numbers=("NWC", "WIO", "NWC"),
        feature_group_count=width,
        preferred_element_type=jnp.float32,
    )


def per_device(history, filter_taps, lengths, inner_gate, values_in, outer_gate, skip_gain):
    position = lax.axis_index("seq")
    n_seq = lax.axis_size("seq")
    requests, tile_len, width = history.shape
    own_tokens = inner_gate.shape[1]
    span_len = own_tokens * n_seq
    assert span_len == tile_len
    chunk = width // CHANNEL_CHUNKS
    product_own = (inner_gate.astype(jnp.float32) * values_in.astype(jnp.float32)).astype(
        jnp.bfloat16
    )
    token_ids = jnp.arange(own_tokens, dtype=jnp.int32)
    exchange = (token_ids[:, None] + token_ids[None, :] == own_tokens - 1).astype(jnp.bfloat16)
    product_own = lax.optimization_barrier(product_own)
    product_rev = jnp.einsum(
        "ik,rkc->ric", exchange, product_own, preferred_element_type=jnp.float32
    ).astype(jnp.bfloat16)
    first_each = [product_rev[:, :, :chunk]] + [
        lax.ppermute(product_rev[:, :, :chunk], "seq", [(d, 0)]) for d in range(1, n_seq)
    ]
    rest_each = [product_rev[:, :, chunk:]] + [
        lax.ppermute(product_rev[:, :, chunk:], "seq", [(d, 0)]) for d in range(1, n_seq)
    ]
    row_ids = position * tile_len + jnp.arange(tile_len, dtype=jnp.int32)
    live_rows = jnp.where(
        (row_ids[None, :] < lengths[:, None])[:, :, None], history, jnp.zeros_like(history)
    )
    prev_keep = ((row_ids - tile_len)[None, :] < lengths[:, None])[:, :, None]

    head_parts = []
    own_parts = []
    scattered = []
    partials = []
    for c in range(CHANNEL_CHUNKS):
        cols = slice(c * chunk, (c + 1) * chunk)
        sent = from_behind(history[:, :, cols], "seq", 1)
        if own_parts:
            (sent, rest_each), _ = lax.optimization_barrier(((sent, rest_each), partials[max(c - 2, 0)]))
            rest_cols = slice((c - 1) * chunk, c * chunk)
            head_first = jnp.concatenate(
                [part[:, :, rest_cols] for part in rest_each[::-1]], axis=1
            )
        else:
            head_first = jnp.concatenate(first_each[::-1], axis=1)
        head_c = jnp.where(position == 0, head_first, sent)
        head_parts.append(head_c)
        prev_live = jnp.where(prev_keep, head_c, jnp.zeros_like(head_c))
        segment = jnp.concatenate([prev_live, live_rows[:, : tile_len - 1, cols]], axis=1)
        if c >= 3 and (c - 2) % 2 == 1:
            segment, _ = lax.optimization_barrier((segment, own_parts[c - 2]))
        partial_rev = correlate(segment, filter_taps[:, cols])
        partials.append(partial_rev)
        blocks = partial_rev.reshape(requests, n_seq, own_tokens, chunk)[:, ::-1]
        if c % 2 == 1 and c != CHANNEL_CHUNKS - 1:
            own_parts.append(send_reduce(blocks, position, n_seq))
            continue
        if c == CHANNEL_CHUNKS - 1:
            half = blocks.shape[3] // 2
            linked = send_reduce(blocks[..., half:], position, n_seq)
            blocks = blocks[..., :half]
        if scattered:
            blocks, _ = lax.optimization_barrier((blocks, scattered[-1]))
        reduced = lax.psum_scatter(blocks, "seq", scatter_dimension=1, tiled=True)
        scattered.append(reduced)
        if c == CHANNEL_CHUNKS - 1:
            own_parts.append(jnp.concatenate([reduced[:, 0], linked], axis=2))
        else:
            own_parts.append(reduced[:, 0])
    summed = jnp.concatenate(own_parts, axis=2)[:, ::-1]
    product_float = product_own.astype(jnp.float32)
    total = summed + skip_gain[None, None, :] * product_float
    mixed = (outer_gate.astype(jnp.float32) * total).astype(jnp.bfloat16)
    next_history = jnp.concatenate(head_parts, axis=2)
    return (mixed, next_history)


def solution(mesh):
    in_specs = (
        P(("group", "batch"), "seq", "chan"),
        P("seq", "chan"),
        P(("group", "batch")),
        P(("group", "batch"), "seq", "chan"),
        P(("group", "batch"), "seq", "chan"),
        P(("group", "batch"), "seq", "chan"),
        P("chan"),
    )
    out_specs = (P(("group", "batch"), "seq", "chan"), P(("group", "batch"), "seq", "chan"))
    return jax.shard_map(
        per_device, mesh=mesh, in_specs=in_specs, out_specs=out_specs, check_vma=False
    )
```

```python
import jax
import jax.numpy as jnp
from jax import lax
from jax.sharding import PartitionSpec as P

CHANNEL_CHUNKS = 4


def from_behind(block, axis, distance):
    devices = range(lax.axis_size(axis))
    route = [(i - distance, i) for i in devices if i - distance in devices]
    return lax.ppermute(block, axis, route)


def correlate(signal, kernel):
    width = signal.shape[2]
    return lax.conv_general_dilated(
        signal,
        kernel[:, None, :],
        (1,),
        "VALID",
        dimension_numbers=("NWC", "WIO", "NWC"),
        feature_group_count=width,
        preferred_element_type=jnp.float32,
    )


def per_device(history, filter_taps, lengths, inner_gate, values_in, outer_gate, skip_gain):
    position = lax.axis_index("seq")
    n_seq = lax.axis_size("seq")
    requests, tile_len, width = history.shape
    own_tokens = inner_gate.shape[1]
    span_len = own_tokens * n_seq
    assert span_len == tile_len
    chunk = width // CHANNEL_CHUNKS
    product_own = (inner_gate.astype(jnp.float32) * values_in.astype(jnp.float32)).astype(
        jnp.bfloat16
    )
    token_ids = jnp.arange(own_tokens, dtype=jnp.int32)
    exchange = (token_ids[:, None] + token_ids[None, :] == own_tokens - 1).astype(jnp.bfloat16)
    product_own = lax.optimization_barrier(product_own)
    product_rev = jnp.einsum(
        "ik,rkc->ric", exchange, product_own, preferred_element_type=jnp.float32
    ).astype(jnp.bfloat16)
    first_each = [product_rev[:, :, :chunk]] + [
        lax.ppermute(product_rev[:, :, :chunk], "seq", [(d, 0)]) for d in range(1, n_seq)
    ]
    rest_each = [product_rev[:, :, chunk:]] + [
        lax.ppermute(product_rev[:, :, chunk:], "seq", [(d, 0)]) for d in range(1, n_seq)
    ]
    row_ids = position * tile_len + jnp.arange(tile_len, dtype=jnp.int32)
    live_rows = jnp.where(
        (row_ids[None, :] < lengths[:, None])[:, :, None], history, jnp.zeros_like(history)
    )
    prev_keep = ((row_ids - tile_len)[None, :] < lengths[:, None])[:, :, None]

    head_parts = []
    own_parts = []
    for c in range(CHANNEL_CHUNKS):
        cols = slice(c * chunk, (c + 1) * chunk)
        sent = from_behind(history[:, :, cols], "seq", 1)
        if own_parts:
            (sent, rest_each), _ = lax.optimization_barrier(((sent, rest_each), last_partial))
            rest_cols = slice((c - 1) * chunk, c * chunk)
            head_first = jnp.concatenate(
                [part[:, :, rest_cols] for part in rest_each[::-1]], axis=1
            )
        else:
            head_first = jnp.concatenate(first_each[::-1], axis=1)
        head_c = jnp.where(position == 0, head_first, sent)
        head_parts.append(head_c)
        prev_live = jnp.where(prev_keep, head_c, jnp.zeros_like(head_c))
        segment = jnp.concatenate([prev_live, live_rows[:, : tile_len - 1, cols]], axis=1)
        partial_rev = correlate(segment, filter_taps[:, cols])
        last_partial = partial_rev
        blocks = partial_rev.reshape(requests, n_seq, own_tokens, chunk)[:, ::-1]
        if own_parts:
            blocks, _ = lax.optimization_barrier((blocks, own_parts[-1]))
        reduced = lax.psum_scatter(blocks, "seq", scatter_dimension=1, tiled=True)
        own_parts.append(reduced[:, 0])
    summed = jnp.einsum(
        "ik,rkc->ric",
        exchange.astype(jnp.float32),
        jnp.concatenate(own_parts, axis=2),
        precision=lax.Precision.HIGHEST,
        preferred_element_type=jnp.float32,
    )
    product_float = product_own.astype(jnp.float32)
    total = summed + skip_gain[None, None, :] * product_float
    mixed = (outer_gate.astype(jnp.float32) * total).astype(jnp.bfloat16)
    next_history = jnp.concatenate(head_parts, axis=2)
    return (mixed, next_history)


def solution(mesh):
    in_specs = (
        P(("group", "batch"), "seq", "chan"),
        P("seq", "chan"),
        P(("group", "batch")),
        P(("group", "batch"), "seq", "chan"),
        P(("group", "batch"), "seq", "chan"),
        P(("group", "batch"), "seq", "chan"),
        P("chan"),
    )
    out_specs = (P(("group", "batch"), "seq", "chan"), P(("group", "batch"), "seq", "chan"))
    return jax.shard_map(
        per_device, mesh=mesh, in_specs=in_specs, out_specs=out_specs, check_vma=False
    )
```

```python
import jax
import jax.numpy as jnp
from jax import lax
from jax.sharding import PartitionSpec as P

CHANNEL_CHUNKS = 4


def from_behind(block, axis, distance):
    devices = range(lax.axis_size(axis))
    route = [(i - distance, i) for i in devices if i - distance in devices]
    return lax.ppermute(block, axis, route)


def correlate(signal, kernel):
    width = signal.shape[2]
    return lax.conv_general_dilated(
        signal,
        kernel[:, None, :],
        (1,),
        "VALID",
        dimension_numbers=("NWC", "WIO", "NWC"),
        feature_group_count=width,
        preferred_element_type=jnp.float32,
    )


def per_device(history, filter_taps, lengths, inner_gate, values_in, outer_gate, skip_gain):
    position = lax.axis_index("seq")
    n_seq = lax.axis_size("seq")
    requests, tile_len, width = history.shape
    own_tokens = inner_gate.shape[1]
    span_len = own_tokens * n_seq
    assert span_len == tile_len
    chunk = width // CHANNEL_CHUNKS
    product_own = (inner_gate.astype(jnp.float32) * values_in.astype(jnp.float32)).astype(
        jnp.bfloat16
    )
    token_ids = jnp.arange(own_tokens, dtype=jnp.int32)
    exchange = (token_ids[:, None] + token_ids[None, :] == own_tokens - 1).astype(jnp.bfloat16)
    product_own = lax.optimization_barrier(product_own)
    product_rev = jnp.einsum(
        "ik,rkc->ric", exchange, product_own, preferred_element_type=jnp.float32
    ).astype(jnp.bfloat16)
    first_each = [product_rev[:, :, :chunk]] + [
        lax.ppermute(product_rev[:, :, :chunk], "seq", [(d, 0)]) for d in range(1, n_seq)
    ]
    rest_each = [product_rev[:, :, chunk:]] + [
        lax.ppermute(product_rev[:, :, chunk:], "seq", [(d, 0)]) for d in range(1, n_seq)
    ]
    row_ids = position * tile_len + jnp.arange(tile_len, dtype=jnp.int32)
    live_rows = jnp.where(
        (row_ids[None, :] < lengths[:, None])[:, :, None], history, jnp.zeros_like(history)
    )
    prev_keep = ((row_ids - tile_len)[None, :] < lengths[:, None])[:, :, None]

    sent_rest = from_behind(history[:, :, chunk:], "seq", 1)
    bounds_rest = [None] + [
        slice(c * chunk - chunk, (c + 1) * chunk - chunk) for c in range(1, CHANNEL_CHUNKS)
    ]
    head_parts = []
    own_parts = []
    for c in range(CHANNEL_CHUNKS):
        cols = slice(c * chunk, (c + 1) * chunk)
        if c == 0:
            sent = from_behind(history[:, :, cols], "seq", 1)
            head_first = jnp.concatenate(first_each[::-1], axis=1)
        else:
            (sent_rest, rest_each), _ = lax.optimization_barrier(((sent_rest, rest_each), last_partial))
            sent = sent_rest[:, :, bounds_rest[c]]
            rest_cols = slice((c - 1) * chunk, c * chunk)
            head_first = jnp.concatenate(
                [part[:, :, rest_cols] for part in rest_each[::-1]], axis=1
            )
        head_c = jnp.where(position == 0, head_first, sent)
        head_parts.append(head_c)
        prev_live = jnp.where(prev_keep, head_c, jnp.zeros_like(head_c))
        segment = jnp.concatenate([prev_live, live_rows[:, : tile_len - 1, cols]], axis=1)
        partial_rev = correlate(segment, filter_taps[:, cols])
        last_partial = partial_rev
        blocks = partial_rev.reshape(requests, n_seq, own_tokens, chunk)[:, ::-1]
        if own_parts:
            blocks, _ = lax.optimization_barrier((blocks, own_parts[-1]))
        reduced = lax.psum_scatter(blocks, "seq", scatter_dimension=1, tiled=True)
        own_parts.append(reduced[:, 0])
    summed = jnp.einsum(
        "ik,rkc->ric",
        exchange.astype(jnp.float32),
        jnp.concatenate(own_parts, axis=2),
        precision=lax.Precision.HIGHEST,
        preferred_element_type=jnp.float32,
    )
    product_float = product_own.astype(jnp.float32)
    total = summed + skip_gain[None, None, :] * product_float
    mixed = (outer_gate.astype(jnp.float32) * total).astype(jnp.bfloat16)
    next_history = jnp.concatenate(head_parts, axis=2)
    return (mixed, next_history)


def solution(mesh):
    in_specs = (
        P(("group", "batch"), "seq", "chan"),
        P("seq", "chan"),
        P(("group", "batch")),
        P(("group", "batch"), "seq", "chan"),
        P(("group", "batch"), "seq", "chan"),
        P(("group", "batch"), "seq", "chan"),
        P("chan"),
    )
    out_specs = (P(("group", "batch"), "seq", "chan"), P(("group", "batch"), "seq", "chan"))
    return jax.shard_map(
        per_device, mesh=mesh, in_specs=in_specs, out_specs=out_specs, check_vma=False
    )
```

```python
import jax
import jax.numpy as jnp
from jax import lax
from jax.sharding import PartitionSpec as P

CHUNK_PARTS = (1, 3, 3, 1)


def from_behind(block, axis, distance):
    devices = range(lax.axis_size(axis))
    route = [(i - distance, i) for i in devices if i - distance in devices]
    return lax.ppermute(block, axis, route)


def correlate(signal, kernel):
    width = signal.shape[2]
    return lax.conv_general_dilated(
        signal,
        kernel[:, None, :],
        (1,),
        "VALID",
        dimension_numbers=("NWC", "WIO", "NWC"),
        feature_group_count=width,
        preferred_element_type=jnp.float32,
    )


def per_device(history, filter_taps, lengths, inner_gate, values_in, outer_gate, skip_gain):
    position = lax.axis_index("seq")
    n_seq = lax.axis_size("seq")
    requests, tile_len, width = history.shape
    own_tokens = inner_gate.shape[1]
    span_len = own_tokens * n_seq
    assert span_len == tile_len
    unit = width // sum(CHUNK_PARTS)
    bounds = [0]
    for parts in CHUNK_PARTS:
        bounds.append(bounds[-1] + parts * unit)
    chunk = bounds[1]
    product_own = (inner_gate.astype(jnp.float32) * values_in.astype(jnp.float32)).astype(
        jnp.bfloat16
    )
    token_ids = jnp.arange(own_tokens, dtype=jnp.int32)
    exchange = (token_ids[:, None] + token_ids[None, :] == own_tokens - 1).astype(jnp.bfloat16)
    product_own = lax.optimization_barrier(product_own)
    product_rev = jnp.einsum(
        "ik,rkc->ric", exchange, product_own, preferred_element_type=jnp.float32
    ).astype(jnp.bfloat16)
    first_each = [product_rev[:, :, :chunk]] + [
        lax.ppermute(product_rev[:, :, :chunk], "seq", [(d, 0)]) for d in range(1, n_seq)
    ]
    rest_each = [product_rev[:, :, chunk:]] + [
        lax.ppermute(product_rev[:, :, chunk:], "seq", [(d, 0)]) for d in range(1, n_seq)
    ]
    row_ids = position * tile_len + jnp.arange(tile_len, dtype=jnp.int32)
    live_rows = jnp.where(
        (row_ids[None, :] < lengths[:, None])[:, :, None], history, jnp.zeros_like(history)
    )
    prev_keep = ((row_ids - tile_len)[None, :] < lengths[:, None])[:, :, None]

    head_parts = []
    own_parts = []
    for c in range(len(CHUNK_PARTS)):
        cols = slice(bounds[c], bounds[c + 1])
        sent = from_behind(history[:, :, cols], "seq", 1)
        if own_parts:
            (sent, rest_each), _ = lax.optimization_barrier(((sent, rest_each), last_partial))
            rest_cols = slice(bounds[c] - chunk, bounds[c + 1] - chunk)
            head_first = jnp.concatenate(
                [part[:, :, rest_cols] for part in rest_each[::-1]], axis=1
            )
        else:
            head_first = jnp.concatenate(first_each[::-1], axis=1)
        head_c = jnp.where(position == 0, head_first, sent)
        head_parts.append(head_c)
        prev_live = jnp.where(prev_keep, head_c, jnp.zeros_like(head_c))
        segment = jnp.concatenate([prev_live, live_rows[:, : tile_len - 1, cols]], axis=1)
        partial_rev = correlate(segment, filter_taps[:, cols])
        last_partial = partial_rev
        blocks = partial_rev.reshape(requests, n_seq, own_tokens, -1)[:, ::-1]
        if own_parts:
            blocks, _ = lax.optimization_barrier((blocks, own_parts[-1]))
        reduced = lax.psum_scatter(blocks, "seq", scatter_dimension=1, tiled=True)
        own_parts.append(reduced[:, 0])
    summed = jnp.einsum(
        "ik,rkc->ric",
        exchange.astype(jnp.float32),
        jnp.concatenate(own_parts, axis=2),
        precision=lax.Precision.HIGHEST,
        preferred_element_type=jnp.float32,
    )
    product_float = product_own.astype(jnp.float32)
    total = summed + skip_gain[None, None, :] * product_float
    mixed = (outer_gate.astype(jnp.float32) * total).astype(jnp.bfloat16)
    next_history = jnp.concatenate(head_parts, axis=2)
    return (mixed, next_history)


def solution(mesh):
    in_specs = (
        P(("group", "batch"), "seq", "chan"),
        P("seq", "chan"),
        P(("group", "batch")),
        P(("group", "batch"), "seq", "chan"),
        P(("group", "batch"), "seq", "chan"),
        P(("group", "batch"), "seq", "chan"),
        P("chan"),
    )
    out_specs = (P(("group", "batch"), "seq", "chan"), P(("group", "batch"), "seq", "chan"))
    return jax.shard_map(
        per_device, mesh=mesh, in_specs=in_specs, out_specs=out_specs, check_vma=False
    )
```

```python
import jax
import jax.numpy as jnp
from jax import lax
from jax.sharding import PartitionSpec as P

CHUNK_PARTS = (3, 3, 2)


def from_behind(block, axis, distance):
    devices = range(lax.axis_size(axis))
    route = [(i - distance, i) for i in devices if i - distance in devices]
    return lax.ppermute(block, axis, route)


def correlate(signal, kernel):
    width = signal.shape[2]
    return lax.conv_general_dilated(
        signal,
        kernel[:, None, :],
        (1,),
        "VALID",
        dimension_numbers=("NWC", "WIO", "NWC"),
        feature_group_count=width,
        preferred_element_type=jnp.float32,
    )


def per_device(history, filter_taps, lengths, inner_gate, values_in, outer_gate, skip_gain):
    position = lax.axis_index("seq")
    n_seq = lax.axis_size("seq")
    requests, tile_len, width = history.shape
    own_tokens = inner_gate.shape[1]
    span_len = own_tokens * n_seq
    assert span_len == tile_len
    unit = width // sum(CHUNK_PARTS)
    bounds = [0]
    for parts in CHUNK_PARTS:
        bounds.append(bounds[-1] + parts * unit)
    chunk = bounds[1]
    product_own = (inner_gate.astype(jnp.float32) * values_in.astype(jnp.float32)).astype(
        jnp.bfloat16
    )
    token_ids = jnp.arange(own_tokens, dtype=jnp.int32)
    exchange = (token_ids[:, None] + token_ids[None, :] == own_tokens - 1).astype(jnp.bfloat16)
    product_own = lax.optimization_barrier(product_own)
    product_rev = jnp.einsum(
        "ik,rkc->ric", exchange, product_own, preferred_element_type=jnp.float32
    ).astype(jnp.bfloat16)
    first_each = [product_rev[:, :, :chunk]] + [
        lax.ppermute(product_rev[:, :, :chunk], "seq", [(d, 0)]) for d in range(1, n_seq)
    ]
    rest_each = [product_rev[:, :, chunk:]] + [
        lax.ppermute(product_rev[:, :, chunk:], "seq", [(d, 0)]) for d in range(1, n_seq)
    ]
    row_ids = position * tile_len + jnp.arange(tile_len, dtype=jnp.int32)
    live_rows = jnp.where(
        (row_ids[None, :] < lengths[:, None])[:, :, None], history, jnp.zeros_like(history)
    )
    prev_keep = ((row_ids - tile_len)[None, :] < lengths[:, None])[:, :, None]

    head_parts = []
    own_parts = []
    for c in range(len(CHUNK_PARTS)):
        cols = slice(bounds[c], bounds[c + 1])
        sent = from_behind(history[:, :, cols], "seq", 1)
        if own_parts:
            (sent, rest_each), _ = lax.optimization_barrier(((sent, rest_each), last_partial))
            rest_cols = slice(bounds[c] - chunk, bounds[c + 1] - chunk)
            head_first = jnp.concatenate(
                [part[:, :, rest_cols] for part in rest_each[::-1]], axis=1
            )
        else:
            head_first = jnp.concatenate(first_each[::-1], axis=1)
        head_c = jnp.where(position == 0, head_first, sent)
        head_parts.append(head_c)
        prev_live = jnp.where(prev_keep, head_c, jnp.zeros_like(head_c))
        segment = jnp.concatenate([prev_live, live_rows[:, : tile_len - 1, cols]], axis=1)
        partial_rev = correlate(segment, filter_taps[:, cols])
        last_partial = partial_rev
        blocks = partial_rev.reshape(requests, n_seq, own_tokens, -1)[:, ::-1]
        if own_parts:
            blocks, _ = lax.optimization_barrier((blocks, own_parts[-1]))
        reduced = lax.psum_scatter(blocks, "seq", scatter_dimension=1, tiled=True)
        own_parts.append(reduced[:, 0])
    summed = jnp.einsum(
        "ik,rkc->ric",
        exchange.astype(jnp.float32),
        jnp.concatenate(own_parts, axis=2),
        precision=lax.Precision.HIGHEST,
        preferred_element_type=jnp.float32,
    )
    product_float = product_own.astype(jnp.float32)
    total = summed + skip_gain[None, None, :] * product_float
    mixed = (outer_gate.astype(jnp.float32) * total).astype(jnp.bfloat16)
    next_history = jnp.concatenate(head_parts, axis=2)
    return (mixed, next_history)


def solution(mesh):
    in_specs = (
        P(("group", "batch"), "seq", "chan"),
        P("seq", "chan"),
        P(("group", "batch")),
        P(("group", "batch"), "seq", "chan"),
        P(("group", "batch"), "seq", "chan"),
        P(("group", "batch"), "seq", "chan"),
        P("chan"),
    )
    out_specs = (P(("group", "batch"), "seq", "chan"), P(("group", "batch"), "seq", "chan"))
    return jax.shard_map(
        per_device, mesh=mesh, in_specs=in_specs, out_specs=out_specs, check_vma=False
    )
```

```python
import jax
import jax.numpy as jnp
from jax import lax
from jax.sharding import PartitionSpec as P

CHUNK_PARTS = (1, 2, 3, 2)


def from_behind(block, axis, distance):
    devices = range(lax.axis_size(axis))
    route = [(i - distance, i) for i in devices if i - distance in devices]
    return lax.ppermute(block, axis, route)


def correlate(signal, kernel):
    width = signal.shape[2]
    return lax.conv_general_dilated(
        signal,
        kernel[:, None, :],
        (1,),
        "VALID",
        dimension_numbers=("NWC", "WIO", "NWC"),
        feature_group_count=width,
        preferred_element_type=jnp.float32,
    )


def per_device(history, filter_taps, lengths, inner_gate, values_in, outer_gate, skip_gain):
    position = lax.axis_index("seq")
    n_seq = lax.axis_size("seq")
    requests, tile_len, width = history.shape
    own_tokens = inner_gate.shape[1]
    span_len = own_tokens * n_seq
    assert span_len == tile_len
    unit = width // sum(CHUNK_PARTS)
    bounds = [0]
    for parts in CHUNK_PARTS:
        bounds.append(bounds[-1] + parts * unit)
    chunk = bounds[1]
    product_own = (inner_gate.astype(jnp.float32) * values_in.astype(jnp.float32)).astype(
        jnp.bfloat16
    )
    token_ids = jnp.arange(own_tokens, dtype=jnp.int32)
    exchange = (token_ids[:, None] + token_ids[None, :] == own_tokens - 1).astype(jnp.bfloat16)
    product_own = lax.optimization_barrier(product_own)
    product_rev = jnp.einsum(
        "ik,rkc->ric", exchange, product_own, preferred_element_type=jnp.float32
    ).astype(jnp.bfloat16)
    first_each = [product_rev[:, :, :chunk]] + [
        lax.ppermute(product_rev[:, :, :chunk], "seq", [(d, 0)]) for d in range(1, n_seq)
    ]
    rest_each = [product_rev[:, :, chunk:]] + [
        lax.ppermute(product_rev[:, :, chunk:], "seq", [(d, 0)]) for d in range(1, n_seq)
    ]
    row_ids = position * tile_len + jnp.arange(tile_len, dtype=jnp.int32)
    live_rows = jnp.where(
        (row_ids[None, :] < lengths[:, None])[:, :, None], history, jnp.zeros_like(history)
    )
    prev_keep = ((row_ids - tile_len)[None, :] < lengths[:, None])[:, :, None]

    head_parts = []
    own_parts = []
    for c in range(len(CHUNK_PARTS)):
        cols = slice(bounds[c], bounds[c + 1])
        sent = from_behind(history[:, :, cols], "seq", 1)
        if own_parts:
            (sent, rest_each), _ = lax.optimization_barrier(((sent, rest_each), last_partial))
            rest_cols = slice(bounds[c] - chunk, bounds[c + 1] - chunk)
            head_first = jnp.concatenate(
                [part[:, :, rest_cols] for part in rest_each[::-1]], axis=1
            )
        else:
            head_first = jnp.concatenate(first_each[::-1], axis=1)
        head_c = jnp.where(position == 0, head_first, sent)
        head_parts.append(head_c)
        prev_live = jnp.where(prev_keep, head_c, jnp.zeros_like(head_c))
        segment = jnp.concatenate([prev_live, live_rows[:, : tile_len - 1, cols]], axis=1)
        partial_rev = correlate(segment, filter_taps[:, cols])
        last_partial = partial_rev
        blocks = partial_rev.reshape(requests, n_seq, own_tokens, -1)[:, ::-1]
        if own_parts:
            blocks, _ = lax.optimization_barrier((blocks, own_parts[-1]))
        reduced = lax.psum_scatter(blocks, "seq", scatter_dimension=1, tiled=True)
        own_parts.append(reduced[:, 0])
    summed = jnp.einsum(
        "ik,rkc->ric",
        exchange.astype(jnp.float32),
        jnp.concatenate(own_parts, axis=2),
        precision=lax.Precision.HIGHEST,
        preferred_element_type=jnp.float32,
    )
    product_float = product_own.astype(jnp.float32)
    total = summed + skip_gain[None, None, :] * product_float
    mixed = (outer_gate.astype(jnp.float32) * total).astype(jnp.bfloat16)
    next_history = jnp.concatenate(head_parts, axis=2)
    return (mixed, next_history)


def solution(mesh):
    in_specs = (
        P(("group", "batch"), "seq", "chan"),
        P("seq", "chan"),
        P(("group", "batch")),
        P(("group", "batch"), "seq", "chan"),
        P(("group", "batch"), "seq", "chan"),
        P(("group", "batch"), "seq", "chan"),
        P("chan"),
    )
    out_specs = (P(("group", "batch"), "seq", "chan"), P(("group", "batch"), "seq", "chan"))
    return jax.shard_map(
        per_device, mesh=mesh, in_specs=in_specs, out_specs=out_specs, check_vma=False
    )
```

```python
import jax
import jax.numpy as jnp
from jax import lax
from jax.sharding import PartitionSpec as P

CHANNEL_CHUNKS = 4


def from_behind(block, axis, distance):
    devices = range(lax.axis_size(axis))
    route = [(i - distance, i) for i in devices if i - distance in devices]
    return lax.ppermute(block, axis, route)


def correlate(signal, kernel):
    width = signal.shape[2]
    return lax.conv_general_dilated(
        signal,
        kernel[:, None, :],
        (1,),
        "VALID",
        dimension_numbers=("NWC", "WIO", "NWC"),
        feature_group_count=width,
        preferred_element_type=jnp.float32,
    )


def per_device(history, filter_taps, lengths, inner_gate, values_in, outer_gate, skip_gain):
    position = lax.axis_index("seq")
    n_seq = lax.axis_size("seq")
    requests, tile_len, width = history.shape
    own_tokens = inner_gate.shape[1]
    span_len = own_tokens * n_seq
    assert span_len == tile_len
    chunk = width // CHANNEL_CHUNKS
    product_own = (inner_gate.astype(jnp.float32) * values_in.astype(jnp.float32)).astype(
        jnp.bfloat16
    )
    token_ids = jnp.arange(own_tokens, dtype=jnp.int32)
    exchange = (token_ids[:, None] + token_ids[None, :] == own_tokens - 1).astype(jnp.bfloat16)
    product_own = lax.optimization_barrier(product_own)
    product_rev = jnp.einsum(
        "ik,rkc->ric", exchange, product_own, preferred_element_type=jnp.float32
    ).astype(jnp.bfloat16)
    first_each = [product_rev[:, :, :chunk]] + [
        lax.ppermute(product_rev[:, :, :chunk], "seq", [(d, 0)]) for d in range(1, n_seq)
    ]
    row_ids = position * tile_len + jnp.arange(tile_len, dtype=jnp.int32)
    live_rows = jnp.where(
        (row_ids[None, :] < lengths[:, None])[:, :, None], history, jnp.zeros_like(history)
    )
    prev_keep = ((row_ids - tile_len)[None, :] < lengths[:, None])[:, :, None]

    head_parts = []
    own_parts = []
    for c in range(CHANNEL_CHUNKS):
        cols = slice(c * chunk, (c + 1) * chunk)
        if c == 0:
            sent = from_behind(history[:, :, cols], "seq", 1)
        else:
            sent = later_sent[c - 1]
        if own_parts:
            (sent, rest_each), _ = lax.optimization_barrier(((sent, rest_each), last_partial))
            rest_cols = slice((c - 1) * chunk, c * chunk)
            head_first = jnp.concatenate(
                [part[:, :, rest_cols] for part in rest_each[::-1]], axis=1
            )
        else:
            head_first = jnp.concatenate(first_each[::-1], axis=1)
        head_c = jnp.where(position == 0, head_first, sent)
        head_parts.append(head_c)
        prev_live = jnp.where(prev_keep, head_c, jnp.zeros_like(head_c))
        segment = jnp.concatenate([prev_live, live_rows[:, : tile_len - 1, cols]], axis=1)
        if c == 0:
            half = chunk // 2
            partial_a = correlate(segment[..., :half], filter_taps[:, :half])
            (rest_src, later_history), _ = lax.optimization_barrier(
                ((product_rev[:, :, chunk:], history[:, :, chunk:]), partial_a)
            )
            rest_each = [rest_src] + [
                lax.ppermute(rest_src, "seq", [(d, 0)]) for d in range(1, n_seq)
            ]
            later_sent = [
                from_behind(later_history[:, :, (k - 1) * chunk : k * chunk], "seq", 1)
                for k in range(1, CHANNEL_CHUNKS)
            ]
            partial_b = correlate(segment[..., half:], filter_taps[:, half:chunk])
            partial_rev = jnp.concatenate([partial_a, partial_b], axis=2)
        else:
            partial_rev = correlate(segment, filter_taps[:, cols])
        last_partial = partial_rev
        blocks = partial_rev.reshape(requests, n_seq, own_tokens, chunk)[:, ::-1]
        if own_parts:
            blocks, _ = lax.optimization_barrier((blocks, own_parts[-1]))
        reduced = lax.psum_scatter(blocks, "seq", scatter_dimension=1, tiled=True)
        own_parts.append(reduced[:, 0])
    summed = jnp.concatenate(own_parts, axis=2)[:, ::-1]
    product_float = product_own.astype(jnp.float32)
    total = summed + skip_gain[None, None, :] * product_float
    mixed = (outer_gate.astype(jnp.float32) * total).astype(jnp.bfloat16)
    next_history = jnp.concatenate(head_parts, axis=2)
    return (mixed, next_history)


def solution(mesh):
    in_specs = (
        P(("group", "batch"), "seq", "chan"),
        P("seq", "chan"),
        P(("group", "batch")),
        P(("group", "batch"), "seq", "chan"),
        P(("group", "batch"), "seq", "chan"),
        P(("group", "batch"), "seq", "chan"),
        P("chan"),
    )
    out_specs = (P(("group", "batch"), "seq", "chan"), P(("group", "batch"), "seq", "chan"))
    return jax.shard_map(
        per_device, mesh=mesh, in_specs=in_specs, out_specs=out_specs, check_vma=False
    )
```

```python
import jax
import jax.numpy as jnp
from jax import lax
from jax.sharding import PartitionSpec as P

CHANNEL_CHUNKS = 4


def from_behind(block, axis, distance):
    devices = range(lax.axis_size(axis))
    route = [(i - distance, i) for i in devices if i - distance in devices]
    return lax.ppermute(block, axis, route)


def correlate(signal, kernel):
    width = signal.shape[2]
    return lax.conv_general_dilated(
        signal,
        kernel[:, None, :],
        (1,),
        "VALID",
        dimension_numbers=("NWC", "WIO", "NWC"),
        feature_group_count=width,
        preferred_element_type=jnp.float32,
    )


def per_device(history, filter_taps, lengths, inner_gate, values_in, outer_gate, skip_gain):
    position = lax.axis_index("seq")
    n_seq = lax.axis_size("seq")
    requests, tile_len, width = history.shape
    own_tokens = inner_gate.shape[1]
    span_len = own_tokens * n_seq
    assert span_len == tile_len
    chunk = width // CHANNEL_CHUNKS
    product_own = (inner_gate.astype(jnp.float32) * values_in.astype(jnp.float32)).astype(
        jnp.bfloat16
    )
    token_ids = jnp.arange(own_tokens, dtype=jnp.int32)
    exchange = (token_ids[:, None] + token_ids[None, :] == own_tokens - 1).astype(jnp.bfloat16)
    product_own = lax.optimization_barrier(product_own)
    product_rev = jnp.einsum(
        "ik,rkc->ric", exchange, product_own, preferred_element_type=jnp.float32
    ).astype(jnp.bfloat16)
    first_each = [product_rev[:, :, :chunk]] + [
        lax.ppermute(product_rev[:, :, :chunk], "seq", [(d, 0)]) for d in range(1, n_seq)
    ]
    rest_each = [product_rev[:, :, chunk:]] + [
        lax.ppermute(product_rev[:, :, chunk:], "seq", [(d, 0)]) for d in range(1, n_seq)
    ]
    row_ids = position * tile_len + jnp.arange(tile_len, dtype=jnp.int32)
    live_rows = jnp.where(
        (row_ids[None, :] < lengths[:, None])[:, :, None], history, jnp.zeros_like(history)
    )
    prev_keep = ((row_ids - tile_len)[None, :] < lengths[:, None])[:, :, None]

    head_parts = []
    own_parts = []
    mixed_parts = []
    for c in range(CHANNEL_CHUNKS):
        cols = slice(c * chunk, (c + 1) * chunk)
        sent = from_behind(history[:, :, cols], "seq", 1)
        if own_parts:
            (sent, rest_each), _ = lax.optimization_barrier(((sent, rest_each), last_partial))
            rest_cols = slice((c - 1) * chunk, c * chunk)
            head_first = jnp.concatenate(
                [part[:, :, rest_cols] for part in rest_each[::-1]], axis=1
            )
        else:
            head_first = jnp.concatenate(first_each[::-1], axis=1)
        head_c = jnp.where(position == 0, head_first, sent)
        head_parts.append(head_c)
        prev_live = jnp.where(prev_keep, head_c, jnp.zeros_like(head_c))
        segment = jnp.concatenate([prev_live, live_rows[:, : tile_len - 1, cols]], axis=1)
        partial_rev = correlate(segment, filter_taps[:, cols])
        last_partial = partial_rev
        blocks = partial_rev.reshape(requests, n_seq, own_tokens, chunk)[:, ::-1]
        if own_parts:
            blocks, _ = lax.optimization_barrier((blocks, own_parts[-1]))
        reduced = lax.psum_scatter(blocks, "seq", scatter_dimension=1, tiled=True)
        own_parts.append(reduced[:, 0])
        total = reduced[:, 0, ::-1] + skip_gain[None, None, cols] * product_own[
            :, :, cols
        ].astype(jnp.float32)
        mixed_parts.append((outer_gate[:, :, cols].astype(jnp.float32) * total).astype(jnp.bfloat16))
    mixed = jnp.concatenate(mixed_parts, axis=2)
    next_history = jnp.concatenate(head_parts, axis=2)
    return (mixed, next_history)


def solution(mesh):
    in_specs = (
        P(("group", "batch"), "seq", "chan"),
        P("seq", "chan"),
        P(("group", "batch")),
        P(("group", "batch"), "seq", "chan"),
        P(("group", "batch"), "seq", "chan"),
        P(("group", "batch"), "seq", "chan"),
        P("chan"),
    )
    out_specs = (P(("group", "batch"), "seq", "chan"), P(("group", "batch"), "seq", "chan"))
    return jax.shard_map(
        per_device, mesh=mesh, in_specs=in_specs, out_specs=out_specs, check_vma=False
    )
```

```python
import jax
import jax.numpy as jnp
from jax import lax
from jax.sharding import PartitionSpec as P

CHANNEL_CHUNKS = 4


def from_behind(block, axis, distance):
    devices = range(lax.axis_size(axis))
    route = [(i - distance, i) for i in devices if i - distance in devices]
    return lax.ppermute(block, axis, route)


def correlate(signal, kernel):
    width = signal.shape[2]
    return lax.conv_general_dilated(
        signal,
        kernel[:, None, :],
        (1,),
        "VALID",
        dimension_numbers=("NWC", "WIO", "NWC"),
        feature_group_count=width,
        preferred_element_type=jnp.float32,
    )


def per_device(history, filter_taps, lengths, inner_gate, values_in, outer_gate, skip_gain):
    position = lax.axis_index("seq")
    n_seq = lax.axis_size("seq")
    requests, tile_len, width = history.shape
    own_tokens = inner_gate.shape[1]
    span_len = own_tokens * n_seq
    assert span_len == tile_len
    chunk = width // CHANNEL_CHUNKS
    product_own = (inner_gate.astype(jnp.float32) * values_in.astype(jnp.float32)).astype(
        jnp.bfloat16
    )
    token_ids = jnp.arange(own_tokens, dtype=jnp.int32)
    exchange = (token_ids[:, None] + token_ids[None, :] == own_tokens - 1).astype(jnp.bfloat16)
    product_own = lax.optimization_barrier(product_own)
    product_rev = jnp.einsum(
        "ik,rkc->ric", exchange, product_own, preferred_element_type=jnp.float32
    ).astype(jnp.bfloat16)
    first_each = [product_rev[:, :, :chunk]] + [
        lax.ppermute(product_rev[:, :, :chunk], "seq", [(d, 0)]) for d in range(1, n_seq)
    ]
    rest_each = [product_rev[:, :, chunk:]] + [
        lax.ppermute(product_rev[:, :, chunk:], "seq", [(d, 0)]) for d in range(1, n_seq)
    ]
    row_ids = position * tile_len + jnp.arange(tile_len, dtype=jnp.int32)
    live_rows = jnp.where(
        (row_ids[None, :] < lengths[:, None])[:, :, None], history, jnp.zeros_like(history)
    )
    prev_keep = ((row_ids - tile_len)[None, :] < lengths[:, None])[:, :, None]

    head_parts = []
    own_parts = []
    for c in range(CHANNEL_CHUNKS):
        cols = slice(c * chunk, (c + 1) * chunk)
        sent = from_behind(history[:, :, cols], "seq", 1)
        if own_parts:
            (sent, rest_each), _ = lax.optimization_barrier(((sent, rest_each), last_partial))
            rest_cols = slice((c - 1) * chunk, c * chunk)
            head_first = jnp.concatenate(
                [part[:, :, rest_cols] for part in rest_each[::-1]], axis=1
            )
        else:
            head_first = jnp.concatenate(first_each[::-1], axis=1)
        head_c = jnp.where(position == 0, head_first, sent)
        head_parts.append(head_c)
        prev_live = jnp.where(prev_keep, head_c, jnp.zeros_like(head_c))
        segment = jnp.concatenate([prev_live, live_rows[:, : tile_len - 1, cols]], axis=1)
        signal = jnp.moveaxis(segment, 0, 1).reshape(1, 2 * tile_len - 1, requests * chunk)
        taps = jnp.tile(filter_taps[:, cols], (1, requests))
        partial_rev = correlate(signal, taps)
        last_partial = partial_rev
        blocks = partial_rev.reshape(n_seq, own_tokens, requests, chunk)[::-1]
        if own_parts:
            blocks, _ = lax.optimization_barrier((blocks, own_parts[-1]))
        reduced = lax.psum_scatter(blocks, "seq", scatter_dimension=0, tiled=True)
        own_parts.append(jnp.moveaxis(reduced[0], 1, 0))
    summed = jnp.concatenate(own_parts, axis=2)[:, ::-1]
    product_float = product_own.astype(jnp.float32)
    total = summed + skip_gain[None, None, :] * product_float
    mixed = (outer_gate.astype(jnp.float32) * total).astype(jnp.bfloat16)
    next_history = jnp.concatenate(head_parts, axis=2)
    return (mixed, next_history)


def solution(mesh):
    in_specs = (
        P(("group", "batch"), "seq", "chan"),
        P("seq", "chan"),
        P(("group", "batch")),
        P(("group", "batch"), "seq", "chan"),
        P(("group", "batch"), "seq", "chan"),
        P(("group", "batch"), "seq", "chan"),
        P("chan"),
    )
    out_specs = (P(("group", "batch"), "seq", "chan"), P(("group", "batch"), "seq", "chan"))
    return jax.shard_map(
        per_device, mesh=mesh, in_specs=in_specs, out_specs=out_specs, check_vma=False
    )
```
